256 devices in a mesh: gx: 8 (over x, core), gy: 4 (over y), gz: 8 (over z).
Axes of the slice: x: 4, y: 4, z: 8, core: 2. Of those that a mesh axis runs over, the one named last changes fastest.
Arguments:
- thermal_state_values: float32 [128, 128, 1024], P('gx', 'gy', 'gz'), may hold values from -6 to 6
- flow_speed_components: float32 [3, 128, 128, 1024], P(None, 'gx', 'gy', 'gz'), may hold values from -14 to 14
- thermal_diffusivity_coefficient: float32 [128, 128, 1024], P('gx', 'gy', 'gz'), may hold values from 0.1 to 3
- specific_volume: float32 [128, 128, 1024], P('gx', 'gy', 'gz'), may hold values from 0.5 to 2
- lower_level_helmholtz_offset: float32 [16, 16, 128], P('gx', 'gy', 'gz'), may hold values from 0.5 to 4
Outputs:
- updated_thermal_state: float32 [128, 128, 1024], P('gx', 'gy', 'gz')
- pressure_iterate_values: float32 [128, 128, 1024], P('gx', 'gy', 'gz')
- pressure_residual: float32 [128, 128, 1024], P('gx', 'gy', 'gz')
The draws below stay inside these ranges and needn't reach their ends.
All inputs are finite; a program needn't handle non-finite values.
Results may differ from the reference program's by a relative error of at most 0.0003.
Values sent between devices are 32-bit elements; how exact they have to be, the bound alone decides.
No kernel may reach another device: no remote copies, remote signals or barrier semaphores. Data moves between devices by JAX's collectives and lax.ppermute only.
A program may use at most 128 MiB of HBM per device.

```python
import math
import jax
import jax.numpy as jnp
from jax import lax

PITERS = 2
SMOOTH = 3
CHEB_C = 8
POINTS_ALONG_X = 128
POINTS_ALONG_Y = 128
POINTS_ALONG_Z = 1024
ELEMENTS_FIRST = 16
ELEMENTS_SECOND = 16
ELEMENTS_THIRD = 128


def node_coord(count):
    node_ids = jnp.arange(count)
    local_pt = (node_ids % 8).astype(jnp.float32)
    element_no = (node_ids // 8).astype(jnp.float32)
    return element_no + 0.5 - 0.5 * jnp.cos(math.pi * local_pt / 7.0)


def draw_flow_speed_components(key, part):
    noise_key, phase_key = jax.random.split(jax.random.fold_in(key, 17))
    coords = (node_coord(POINTS_ALONG_X)[:, None, None], node_coord(POINTS_ALONG_Y)[None, :, None], node_coord(POINTS_ALONG_Z)[None, None, :])
    phases = jax.random.uniform(phase_key, (6,), jnp.float32, 0.0, 2.0 * math.pi)
    noise = 2.0 * jax.random.truncated_normal(noise_key, -4.0, 4.0, (3, POINTS_ALONG_X, POINTS_ALONG_Y, POINTS_ALONG_Z), jnp.float32)
    amplitude = 4.0
    wave_num = 2.0 * math.pi / 6.0
    components = []
    for direction_index in range(3):
        along = jnp.sin(wave_num * coords[direction_index] + phases[direction_index])
        across = 1.0 + 0.5 * jnp.sin(wave_num * coords[(direction_index + 1) % 3] + phases[direction_index + 3])
        components.append(jnp.broadcast_to(amplitude * along * across, (POINTS_ALONG_X, POINTS_ALONG_Y, POINTS_ALONG_Z)))
    return noise + jnp.stack(components)


def block_scale(rng, dims, cuts, smallest, top_value):
    def one(dim, shards_of):
        heights = jax.random.uniform(jax.random.fold_in(jax.random.fold_in(rng, 6), dim), (shards_of,), jnp.float32, smallest / len(cuts), top_value / len(cuts))
        return jnp.repeat(jnp.exp(heights), dims[dim] // shards_of).reshape((-1,) + (1,) * (len(dims) - dim - 1))

    gain = one(*cuts[0])
    for cut in cuts[1:]:
        gain = gain * one(*cut)
    return gain


def gaussian(rng, dims, deviation, bound, pieces=(), kind=jnp.bfloat16):
    entries = deviation * jax.random.normal(rng, dims, jnp.float32)
    if pieces:
        entries = entries * block_scale(rng, dims, pieces, -0.22, 0.18)
    return jnp.clip(entries, -bound, bound).astype(kind)


def setup_inputs(seed: int = 0) -> dict:
    seeds = jax.random.split(jax.random.key(seed), 6)
    return {
        "thermal_state_values": gaussian(seeds[0], (POINTS_ALONG_X, POINTS_ALONG_Y, POINTS_ALONG_Z), 1.0, 6.0, ((0, 8), (1, 4), (2, 8)), jnp.float32),
        "flow_speed_components": draw_flow_speed_components(jax.random.fold_in(seeds[5], 71), 0),
        "thermal_diffusivity_coefficient": jnp.clip(jnp.exp(math.log(3.0) - 3.4011974 * jax.random.uniform(seeds[2], (POINTS_ALONG_X, POINTS_ALONG_Y, POINTS_ALONG_Z), jnp.float32) ** block_scale(seeds[2], (POINTS_ALONG_X, POINTS_ALONG_Y, POINTS_ALONG_Z), ((0, 8), (1, 4), (2, 8)), -0.2, 0.2)), 0.1, 3.0),
        "specific_volume": jnp.clip(jnp.exp(math.log(2.0) - 1.3862944 * jax.random.uniform(seeds[3], (POINTS_ALONG_X, POINTS_ALONG_Y, POINTS_ALONG_Z), jnp.float32) ** block_scale(seeds[3], (POINTS_ALONG_X, POINTS_ALONG_Y, POINTS_ALONG_Z), ((0, 8), (1, 4), (2, 8)), -0.2, 0.2)), 0.5, 2.0),
        "lower_level_helmholtz_offset": jnp.clip(jnp.exp(math.log(4.0) - 2.0794415 * jax.random.uniform(seeds[4], (ELEMENTS_FIRST, ELEMENTS_SECOND, ELEMENTS_THIRD), jnp.float32) ** block_scale(seeds[4], (ELEMENTS_FIRST, ELEMENTS_SECOND, ELEMENTS_THIRD), ((0, 8), (1, 4), (2, 8)), -0.2, 0.2)), 0.5, 4.0),
    }


CLOCK_STEP_SIZE = 0.0002
HELM_SHIFT = 1.0
FINE_LOW = 0.25
FINE_HIGH = 3.0
COARSE_LOW = 0.07
COARSE_HIGH = 2.0
GLL_POINTS = (-1.0, -0.8717401485096066, -0.5917001814331423, -0.2092992179024789, 0.0, 0.2092992179024789, 0.5917001814331423, 0.8717401485096066, 1.0)


def legendre_seven(point):
    p_prev = 1.0
    p_cur = point
    for order_k in range(1, 7):
        p_next = ((2.0 * order_k + 1.0) * point * p_cur - order_k * p_prev) / (order_k + 1.0)
        p_prev = p_cur
        p_cur = p_next
    return p_cur


def gll_tables():
    degree_n = 7
    points = list(GLL_POINTS[:4] + GLL_POINTS[5:])
    legend = [legendre_seven(point) for point in points]
    weights = [2.0 / (degree_n * (degree_n + 1) * value * value) for value in legend]
    derivs = []
    for row_no in range(8):
        row_vals = []
        for col_no in range(8):
            if row_no != col_no:
                row_vals.append(legend[row_no] / (legend[col_no] * (points[row_no] - points[col_no])))
            else:
                row_vals.append(0.0)
        derivs.append(row_vals)
    derivs[0][0] = -degree_n * (degree_n + 1) / 4.0
    derivs[7][7] = degree_n * (degree_n + 1) / 4.0
    return jnp.asarray(derivs, jnp.float32), jnp.asarray(weights, jnp.float32)


def weight_cube(weights):
    return weights[:, None, None] * weights[None, :, None] * weights[None, None, :]


def pair_pass(padded, direction_index):
    extent = padded.shape[direction_index]
    zero_rim = jnp.zeros_like(lax.slice_in_dim(padded, 0, 1, axis=direction_index))
    shifted_up = jnp.concatenate([lax.slice_in_dim(padded, 1, extent, axis=direction_index), zero_rim], axis=direction_index)
    shifted_down = jnp.concatenate([zero_rim, lax.slice_in_dim(padded, 0, extent - 1, axis=direction_index)], axis=direction_index)
    position = lax.broadcasted_iota(jnp.int32, padded.shape, direction_index) % 8
    return padded + jnp.where(position == 0, shifted_up, 0.0) + jnp.where(position == 1, shifted_down, 0.0)


def assemble(values):
    padded = jnp.pad(values, 1)
    for direction_index in range(3):
        padded = pair_pass(padded, direction_index)
    return padded[1:-1, 1:-1, 1:-1]


def apply_derivative_matrix(values, small_t, direction_index):
    full_shape = values.shape
    blocks = values.reshape(full_shape[:direction_index] + (full_shape[direction_index] // 8, 8) + full_shape[direction_index + 1:])
    result = jnp.tensordot(blocks, small_t, axes=([direction_index + 1], [1]), precision=lax.Precision.HIGHEST)
    return jnp.moveaxis(result, -1, direction_index + 1).reshape(full_shape)


def stencil(padded, shift_c):
    centre = padded[1:-1, 1:-1, 1:-1]
    beside_all = padded[2:, 1:-1, 1:-1] + padded[:-2, 1:-1, 1:-1]
    beside_all = beside_all + padded[1:-1, 2:, 1:-1] + padded[1:-1, :-2, 1:-1]
    beside_all = beside_all + padded[1:-1, 1:-1, 2:] + padded[1:-1, 1:-1, :-2]
    return (6.0 + shift_c) * centre - beside_all


def chebyshev(equation_misfit, apply_fn, inv_diag, low_end, high_end, sweeps, keep_resid):
    centre = 0.5 * (high_end + low_end)
    half_span = 0.5 * (high_end - low_end)
    span_ratio = centre / half_span
    rho_old = 1.0 / span_ratio
    direction = (equation_misfit * inv_diag) * (1.0 / centre)
    solution = direction
    for sweep_no in range(1, sweeps):
        equation_misfit = equation_misfit - apply_fn(direction)
        rho_new = 1.0 / (2.0 * span_ratio - rho_old)
        direction = (rho_new * rho_old) * direction + (2.0 * rho_new / half_span) * (equation_misfit * inv_diag)
        solution = solution + direction
        rho_old = rho_new
    if keep_resid:
        equation_misfit = equation_misfit - apply_fn(direction)
    return solution, equation_misfit


def reference(thermal_state_values, flow_speed_components, thermal_diffusivity_coefficient, specific_volume, lower_level_helmholtz_offset):
    derivs, weights = gll_tables()
    interpolation_apply = derivs
    adjoint_interpolation = derivs.T
    square_back = (derivs * derivs).T
    cube_w = weight_cube(weights)
    count_x, count_y, count_z = lower_level_helmholtz_offset.shape
    quadrature_coefficient = jnp.tile(cube_w, (count_x, count_y, count_z))
    quadrature_lumped_matrix = assemble(quadrature_coefficient)
    partial_derivative_stack = [apply_derivative_matrix(thermal_state_values, interpolation_apply, direction_index) for direction_index in range(3)]
    advect = flow_speed_components[0] * partial_derivative_stack[0] + flow_speed_components[1] * partial_derivative_stack[1] + flow_speed_components[2] * partial_derivative_stack[2]
    diffuse = apply_derivative_matrix(quadrature_coefficient * thermal_diffusivity_coefficient * partial_derivative_stack[0], adjoint_interpolation, 0)
    diffuse = diffuse + apply_derivative_matrix(quadrature_coefficient * thermal_diffusivity_coefficient * partial_derivative_stack[1], adjoint_interpolation, 1)
    diffuse = diffuse + apply_derivative_matrix(quadrature_coefficient * thermal_diffusivity_coefficient * partial_derivative_stack[2], adjoint_interpolation, 2)
    volumetric_source_strength = assemble(-(quadrature_coefficient * advect) - diffuse)
    updated_thermal_state = thermal_state_values + CLOCK_STEP_SIZE * volumetric_source_strength / quadrature_lumped_matrix
    boundary_heat_outflow = apply_derivative_matrix(quadrature_coefficient * flow_speed_components[0], adjoint_interpolation, 0) + apply_derivative_matrix(quadrature_coefficient * flow_speed_components[1], adjoint_interpolation, 1)
    boundary_heat_outflow = boundary_heat_outflow + apply_derivative_matrix(quadrature_coefficient * (flow_speed_components[2] + updated_thermal_state), adjoint_interpolation, 2)
    right_side = assemble(boundary_heat_outflow)
    coef_w = quadrature_coefficient * specific_volume
    jacobi = assemble(apply_derivative_matrix(coef_w, square_back, 0) + apply_derivative_matrix(coef_w, square_back, 1) + apply_derivative_matrix(coef_w, square_back, 2) + HELM_SHIFT * quadrature_coefficient)
    inv_jac = 1.0 / jacobi

    def apply_fine(values):
        local_k = apply_derivative_matrix(coef_w * apply_derivative_matrix(values, interpolation_apply, 0), adjoint_interpolation, 0)
        local_k = local_k + apply_derivative_matrix(coef_w * apply_derivative_matrix(values, interpolation_apply, 1), adjoint_interpolation, 1)
        local_k = local_k + apply_derivative_matrix(coef_w * apply_derivative_matrix(values, interpolation_apply, 2), adjoint_interpolation, 2)
        return assemble(local_k + HELM_SHIFT * quadrature_coefficient * values)

    def apply_coarse(values):
        return stencil(jnp.pad(values, 1), lower_level_helmholtz_offset)

    coarse_inv = 1.0 / (6.0 + lower_level_helmholtz_offset)
    pressure_iterate_values = jnp.zeros_like(thermal_state_values)
    equation_misfit = right_side
    for iter_no in range(PITERS):
        smooth, resid_s = chebyshev(equation_misfit, apply_fine, inv_jac, FINE_LOW, FINE_HIGH, SMOOTH, True)
        coarse_r = (quadrature_coefficient * resid_s).reshape(count_x, 8, count_y, 8, count_z, 8).sum(axis=(1, 3, 5)) / 8.0
        correct, unused = chebyshev(coarse_r, apply_coarse, coarse_inv, COARSE_LOW, COARSE_HIGH, CHEB_C, False)
        expanded = jnp.repeat(jnp.repeat(jnp.repeat(correct, 8, 0), 8, 1), 8, 2)
        prolong = assemble(quadrature_coefficient * expanded) / quadrature_lumped_matrix
        pressure_iterate_values = pressure_iterate_values + smooth + prolong
        equation_misfit = resid_s - apply_fine(prolong)
    return updated_thermal_state, pressure_iterate_values, equation_misfit
```

```python
import jax
import jax.numpy as jnp
from jax import lax
from jax.sharding import PartitionSpec as P
import numpy as np

PITERS = 2
SMOOTH = 3
CHEB_C = 8


CLOCK_STEP_SIZE = 0.0002
HELM_SHIFT = 1.0
FINE_LOW = 0.25
FINE_HIGH = 3.0
COARSE_LOW = 0.07
COARSE_HIGH = 2.0
GLL_POINTS = (
    -1.0,
    -0.8717401485096066,
    -0.5917001814331423,
    -0.2092992179024789,
    0.0,
    0.2092992179024789,
    0.5917001814331423,
    0.8717401485096066,
    1.0,
)


def legendre_seven(point):
    p_prev = 1.0
    p_cur = point
    for order_k in range(1, 7):
        p_next = ((2.0 * order_k + 1.0) * point * p_cur - order_k * p_prev) / (order_k + 1.0)
        p_prev = p_cur
        p_cur = p_next
    return p_cur


def gll_tables():
    degree_n = 7
    points = list(GLL_POINTS[:4] + GLL_POINTS[5:])
    legend = [legendre_seven(point) for point in points]
    weights = [2.0 / (degree_n * (degree_n + 1) * value * value) for value in legend]
    derivs = []
    for row_no in range(8):
        row_vals = []
        for col_no in range(8):
            if row_no != col_no:
                row_vals.append(
                    legend[row_no] / (legend[col_no] * (points[row_no] - points[col_no]))
                )
            else:
                row_vals.append(0.0)
        derivs.append(row_vals)
    derivs[0][0] = -degree_n * (degree_n + 1) / 4.0
    derivs[7][7] = degree_n * (degree_n + 1) / 4.0
    return (jnp.asarray(derivs, jnp.float32), jnp.asarray(weights, jnp.float32))


def weight_cube(weights):
    return weights[:, None, None] * weights[None, :, None] * weights[None, None, :]


def pair_pass(padded, direction_index):
    extent = padded.shape[direction_index]
    zero_rim = jnp.zeros_like(lax.slice_in_dim(padded, 0, 1, axis=direction_index))
    shifted_up = jnp.concatenate(
        [lax.slice_in_dim(padded, 1, extent, axis=direction_index), zero_rim], axis=direction_index
    )
    shifted_down = jnp.concatenate(
        [zero_rim, lax.slice_in_dim(padded, 0, extent - 1, axis=direction_index)],
        axis=direction_index,
    )
    position = lax.broadcasted_iota(jnp.int32, padded.shape, direction_index) % 8
    return (
        padded
        + jnp.where(position == 0, shifted_up, 0.0)
        + jnp.where(position == 1, shifted_down, 0.0)
    )


def make_pair(small_t, length_along_z):
    band_t = jnp.kron(jnp.eye(length_along_z // 8, dtype=jnp.float32), small_t).T
    return (small_t, band_t)


def apply_derivative_matrix(values, tables, direction_index):
    small_t, band_t = tables
    length_along_x, length_along_y, length_along_z = values.shape
    if direction_index == 0:
        blocks = values.reshape(length_along_x // 8, 8, length_along_y * length_along_z)
        result = jnp.einsum("ia,xar->xir", small_t, blocks, precision=lax.Precision.HIGHEST)
        return result.reshape(values.shape)
    if direction_index == 1:
        blocks = values.reshape(length_along_x, length_along_y // 8, 8, length_along_z)
        result = jnp.einsum("ia,pyaz->pyiz", small_t, blocks, precision=lax.Precision.HIGHEST)
        return result.reshape(values.shape)
    result = jnp.dot(
        values.reshape(length_along_x * length_along_y, length_along_z),
        band_t,
        precision=lax.Precision.HIGHEST,
    )
    return result.reshape(values.shape)


def stencil(padded, shift_c):
    centre = padded[1:-1, 1:-1, 1:-1]
    beside_all = padded[2:, 1:-1, 1:-1] + padded[:-2, 1:-1, 1:-1]
    beside_all = beside_all + padded[1:-1, 2:, 1:-1] + padded[1:-1, :-2, 1:-1]
    beside_all = beside_all + padded[1:-1, 1:-1, 2:] + padded[1:-1, 1:-1, :-2]
    return (6.0 + shift_c) * centre - beside_all


def chebyshev(equation_misfit, apply_fn, inv_diag, low_end, high_end, sweeps, keep_resid):
    centre = 0.5 * (high_end + low_end)
    half_span = 0.5 * (high_end - low_end)
    span_ratio = centre / half_span
    rho_old = 1.0 / span_ratio
    direction = equation_misfit * inv_diag * (1.0 / centre)
    solution = direction
    for sweep_no in range(1, sweeps):
        equation_misfit = equation_misfit - apply_fn(direction)
        rho_new = 1.0 / (2.0 * span_ratio - rho_old)
        direction = rho_new * rho_old * direction + 2.0 * rho_new / half_span * (
            equation_misfit * inv_diag
        )
        solution = solution + direction
        rho_old = rho_new
    if keep_resid:
        equation_misfit = equation_misfit - apply_fn(direction)
    return (solution, equation_misfit)


AXES = ("gx", "gy", "gz")
OFFSETS = tuple(
    (ox, oy, oz)
    for ox in (-1, 0, 1)
    for oy in (-1, 0, 1)
    for oz in (-1, 0, 1)
    if (ox, oy, oz) != (0, 0, 0)
)


def neighbour_pairs(offset, sizes):
    def lin(c):
        return (c[0] * sizes[1] + c[1]) * sizes[2] + c[2]

    pairs = []
    for i in range(sizes[0]):
        for j in range(sizes[1]):
            for k in range(sizes[2]):
                dst = (i - offset[0], j - offset[1], k - offset[2])
                if all(0 <= dst[d] < sizes[d] for d in range(3)):
                    pairs.append((lin((i, j, k)), lin(dst)))
    return pairs


def side_region(values, sides):
    for dim, side in zip((1, 2, 3), sides):
        extent = values.shape[dim]
        if side == 1:
            values = lax.slice_in_dim(values, extent - 1, extent, axis=dim)
        elif side == -1:
            values = lax.slice_in_dim(values, 0, 1, axis=dim)
    return values


def halo_pad(values, sizes):
    pieces = {}
    for offset in OFFSETS:
        piece = side_region(values, tuple(-o for o in offset))
        pairs = neighbour_pairs(offset, sizes)
        if pairs:
            pieces[offset] = lax.ppermute(piece, AXES, pairs)
        else:
            pieces[offset] = jnp.zeros_like(piece)
    pieces[(0, 0, 0)] = values
    planes = []
    for ox in (-1, 0, 1):
        rows = []
        for oy in (-1, 0, 1):
            rows.append(jnp.concatenate([pieces[(ox, oy, oz)] for oz in (-1, 0, 1)], axis=3))
        planes.append(jnp.concatenate(rows, axis=2))
    return jnp.concatenate(planes, axis=1)


def assemble_padded(padded):
    for direction_index in range(1, 4):
        padded = pair_pass(padded, direction_index)
    return padded[:, 1:-1, 1:-1, 1:-1]


def assemble_many(stack, sizes):
    return assemble_padded(halo_pad(stack, sizes))


def gather_coarse(values, sizes):
    gathered = lax.all_gather(values, AXES, axis=0, tiled=False)
    ex, ey, ez = values.shape
    gathered = gathered.reshape(sizes[0], sizes[1], sizes[2], ex, ey, ez)
    gathered = gathered.transpose(0, 3, 1, 4, 2, 5)
    return gathered.reshape(sizes[0] * ex, sizes[1] * ey, sizes[2] * ez)


def shards(sizes):
    def body(
        thermal_state_values,
        flow_speed_components,
        thermal_diffusivity_coefficient,
        specific_volume,
        lower_level_helmholtz_offset,
    ):
        derivs, weights = gll_tables()
        length_along_x, length_along_y, length_along_z = thermal_state_values.shape
        blocks_x, blocks_y, blocks_z = lower_level_helmholtz_offset.shape
        interpolation_apply = make_pair(derivs, length_along_z)
        adjoint_interpolation = make_pair(derivs.T, length_along_z)
        square_back = make_pair((derivs * derivs).T, length_along_z)
        cube_w = weight_cube(weights)
        quadrature_coefficient = jnp.tile(cube_w, (blocks_x, blocks_y, blocks_z))

        def assemble_one(values):
            return assemble_many(values[None], sizes)[0]

        helm_full = gather_coarse(lower_level_helmholtz_offset, sizes)
        ix = lax.axis_index("gx")
        iy = lax.axis_index("gy")
        iz = lax.axis_index("gz")

        def padded_weights(length):
            return weights[np.arange(7, 7 + length + 2) % 8]

        w_pad = (
            padded_weights(length_along_x)[:, None, None]
            * padded_weights(length_along_y)[None, :, None]
        ) * padded_weights(length_along_z)[None, None, :]

        def assemble_from_coarse(coarse_full):
            coarse_pad = jnp.pad(coarse_full, 1)
            window = lax.dynamic_slice(
                coarse_pad,
                (ix * blocks_x, iy * blocks_y, iz * blocks_z),
                (blocks_x + 2, blocks_y + 2, blocks_z + 2),
            )
            nodes = jnp.repeat(jnp.repeat(jnp.repeat(window, 8, 0), 8, 1), 8, 2)
            nodes = nodes[
                7 : 7 + length_along_x + 2, 7 : 7 + length_along_y + 2, 7 : 7 + length_along_z + 2
            ]
            return assemble_padded((w_pad * nodes)[None])[0]

        quadrature_lumped_matrix = assemble_from_coarse(
            jnp.ones(helm_full.shape, jnp.float32)
        )

        partial_derivative_stack = [
            apply_derivative_matrix(thermal_state_values, interpolation_apply, direction_index)
            for direction_index in range(3)
        ]
        advect = (
            flow_speed_components[0] * partial_derivative_stack[0]
            + flow_speed_components[1] * partial_derivative_stack[1]
            + flow_speed_components[2] * partial_derivative_stack[2]
        )
        diffuse = apply_derivative_matrix(
            quadrature_coefficient * thermal_diffusivity_coefficient * partial_derivative_stack[0],
            adjoint_interpolation,
            0,
        )
        diffuse = diffuse + apply_derivative_matrix(
            quadrature_coefficient * thermal_diffusivity_coefficient * partial_derivative_stack[1],
            adjoint_interpolation,
            1,
        )
        diffuse = diffuse + apply_derivative_matrix(
            quadrature_coefficient * thermal_diffusivity_coefficient * partial_derivative_stack[2],
            adjoint_interpolation,
            2,
        )
        heat_local = -(quadrature_coefficient * advect) - diffuse
        coef_w = quadrature_coefficient * specific_volume
        jacobi_local = (
            apply_derivative_matrix(coef_w, square_back, 0)
            + apply_derivative_matrix(coef_w, square_back, 1)
            + apply_derivative_matrix(coef_w, square_back, 2)
            + HELM_SHIFT * quadrature_coefficient
        )
        both = assemble_many(jnp.stack([heat_local, jacobi_local]), sizes)
        volumetric_source_strength = both[0]
        jacobi = both[1]
        updated_thermal_state = (
            thermal_state_values
            + CLOCK_STEP_SIZE * volumetric_source_strength / quadrature_lumped_matrix
        )
        boundary_heat_outflow = apply_derivative_matrix(
            quadrature_coefficient * flow_speed_components[0], adjoint_interpolation, 0
        ) + apply_derivative_matrix(
            quadrature_coefficient * flow_speed_components[1], adjoint_interpolation, 1
        )
        boundary_heat_outflow = boundary_heat_outflow + apply_derivative_matrix(
            quadrature_coefficient * (flow_speed_components[2] + updated_thermal_state),
            adjoint_interpolation,
            2,
        )
        right_side = assemble_one(boundary_heat_outflow)
        inv_jac = 1.0 / jacobi

        def apply_fine(values):
            local_k = apply_derivative_matrix(
                coef_w * apply_derivative_matrix(values, interpolation_apply, 0),
                adjoint_interpolation,
                0,
            )
            local_k = local_k + apply_derivative_matrix(
                coef_w * apply_derivative_matrix(values, interpolation_apply, 1),
                adjoint_interpolation,
                1,
            )
            local_k = local_k + apply_derivative_matrix(
                coef_w * apply_derivative_matrix(values, interpolation_apply, 2),
                adjoint_interpolation,
                2,
            )
            return assemble_one(local_k + HELM_SHIFT * quadrature_coefficient * values)

        def apply_coarse(values):
            return stencil(jnp.pad(values, 1), helm_full)

        coarse_inv = 1.0 / (6.0 + helm_full)
        row_ids = lax.broadcasted_iota(jnp.int32, (length_along_z, blocks_z), 0) // 8
        col_ids = lax.broadcasted_iota(jnp.int32, (length_along_z, blocks_z), 1)
        summer = jnp.where(row_ids == col_ids, 1.0, 0.0).astype(jnp.float32)
        pressure_iterate_values = jnp.zeros_like(thermal_state_values)
        equation_misfit = right_side
        for iter_no in range(PITERS):
            smooth, resid_s = chebyshev(
                equation_misfit, apply_fine, inv_jac, FINE_LOW, FINE_HIGH, SMOOTH, True
            )
            along_z = jnp.dot(
                (quadrature_coefficient * resid_s).reshape(
                    length_along_x * length_along_y, length_along_z
                ),
                summer,
                precision=lax.Precision.HIGHEST,
            )
            coarse_r = along_z.reshape(blocks_x, 8, blocks_y, 8, blocks_z).sum(axis=(1, 3)) / 8.0
            coarse_full = gather_coarse(coarse_r, sizes)
            correct, unused = chebyshev(
                coarse_full, apply_coarse, coarse_inv, COARSE_LOW, COARSE_HIGH, CHEB_C, False
            )
            prolong = assemble_from_coarse(correct) / quadrature_lumped_matrix
            pressure_iterate_values = pressure_iterate_values + smooth + prolong
            equation_misfit = resid_s - apply_fine(prolong)
        return (updated_thermal_state, pressure_iterate_values, equation_misfit)

    return body


def solution(mesh):
    sizes = tuple(mesh.shape[name] for name in AXES)
    in_specs = (
        P("gx", "gy", "gz"),
        P(None, "gx", "gy", "gz"),
        P("gx", "gy", "gz"),
        P("gx", "gy", "gz"),
        P("gx", "gy", "gz"),
    )
    out_specs = (P("gx", "gy", "gz"), P("gx", "gy", "gz"), P("gx", "gy", "gz"))
    return jax.shard_map(
        shards(sizes), mesh=mesh, in_specs=in_specs, out_specs=out_specs, check_vma=False
    )
```

```python
import jax
import jax.numpy as jnp
from jax import lax
from jax.sharding import PartitionSpec as P
import numpy as np

PITERS = 2
SMOOTH = 3
CHEB_C = 8


CLOCK_STEP_SIZE = 0.0002
HELM_SHIFT = 1.0
FINE_LOW = 0.25
FINE_HIGH = 3.0
COARSE_LOW = 0.07
COARSE_HIGH = 2.0
GLL_POINTS = (
    -1.0,
    -0.8717401485096066,
    -0.5917001814331423,
    -0.2092992179024789,
    0.0,
    0.2092992179024789,
    0.5917001814331423,
    0.8717401485096066,
    1.0,
)


def legendre_seven(point):
    p_prev = 1.0
    p_cur = point
    for order_k in range(1, 7):
        p_next = ((2.0 * order_k + 1.0) * point * p_cur - order_k * p_prev) / (order_k + 1.0)
        p_prev = p_cur
        p_cur = p_next
    return p_cur


def gll_tables():
    degree_n = 7
    points = list(GLL_POINTS[:4] + GLL_POINTS[5:])
    legend = [legendre_seven(point) for point in points]
    weights = [2.0 / (degree_n * (degree_n + 1) * value * value) for value in legend]
    derivs = []
    for row_no in range(8):
        row_vals = []
        for col_no in range(8):
            if row_no != col_no:
                row_vals.append(
                    legend[row_no] / (legend[col_no] * (points[row_no] - points[col_no]))
                )
            else:
                row_vals.append(0.0)
        derivs.append(row_vals)
    derivs[0][0] = -degree_n * (degree_n + 1) / 4.0
    derivs[7][7] = degree_n * (degree_n + 1) / 4.0
    return (jnp.asarray(derivs, jnp.float32), jnp.asarray(weights, jnp.float32))


def weight_cube(weights):
    return weights[:, None, None] * weights[None, :, None] * weights[None, None, :]


def pair_pass(padded, direction_index):
    extent = padded.shape[direction_index]
    zero_rim = jnp.zeros_like(lax.slice_in_dim(padded, 0, 1, axis=direction_index))
    shifted_up = jnp.concatenate(
        [lax.slice_in_dim(padded, 1, extent, axis=direction_index), zero_rim], axis=direction_index
    )
    shifted_down = jnp.concatenate(
        [zero_rim, lax.slice_in_dim(padded, 0, extent - 1, axis=direction_index)],
        axis=direction_index,
    )
    position = lax.broadcasted_iota(jnp.int32, padded.shape, direction_index) % 8
    return (
        padded
        + jnp.where(position == 0, shifted_up, 0.0)
        + jnp.where(position == 1, shifted_down, 0.0)
    )


def make_pair(small_t, length_along_z):
    band_t = jnp.kron(jnp.eye(length_along_z // 8, dtype=jnp.float32), small_t).T
    return (small_t, band_t)


def apply_derivative_matrix(values, tables, direction_index):
    small_t, band_t = tables
    length_along_x, length_along_y, length_along_z = values.shape
    if direction_index == 0:
        blocks = values.reshape(length_along_x // 8, 8, length_along_y * length_along_z)
        result = jnp.einsum("ia,xar->xir", small_t, blocks, precision=lax.Precision.HIGHEST)
        return result.reshape(values.shape)
    if direction_index == 1:
        blocks = values.reshape(length_along_x, length_along_y // 8, 8, length_along_z)
        result = jnp.einsum("ia,pyaz->pyiz", small_t, blocks, precision=lax.Precision.HIGHEST)
        return result.reshape(values.shape)
    result = jnp.dot(
        values.reshape(length_along_x * length_along_y, length_along_z),
        band_t,
        precision=lax.Precision.HIGHEST,
    )
    return result.reshape(values.shape)


def stencil(padded, shift_c):
    centre = padded[1:-1, 1:-1, 1:-1]
    beside_all = padded[2:, 1:-1, 1:-1] + padded[:-2, 1:-1, 1:-1]
    beside_all = beside_all + padded[1:-1, 2:, 1:-1] + padded[1:-1, :-2, 1:-1]
    beside_all = beside_all + padded[1:-1, 1:-1, 2:] + padded[1:-1, 1:-1, :-2]
    return (6.0 + shift_c) * centre - beside_all


def chebyshev(equation_misfit, apply_fn, inv_diag, low_end, high_end, sweeps, keep_resid):
    centre = 0.5 * (high_end + low_end)
    half_span = 0.5 * (high_end - low_end)
    span_ratio = centre / half_span
    rho_old = 1.0 / span_ratio
    direction = equation_misfit * inv_diag * (1.0 / centre)
    solution = direction
    for sweep_no in range(1, sweeps):
        equation_misfit = equation_misfit - apply_fn(direction)
        rho_new = 1.0 / (2.0 * span_ratio - rho_old)
        direction = rho_new * rho_old * direction + 2.0 * rho_new / half_span * (
            equation_misfit * inv_diag
        )
        solution = solution + direction
        rho_old = rho_new
    if keep_resid:
        equation_misfit = equation_misfit - apply_fn(direction)
    return (solution, equation_misfit)


def extended(cells, sides, width):
    for axis, dim in sides:
        count = lax.axis_size(axis)
        ends = count - 1
        head = lax.slice_in_dim(cells, 0, width, axis=dim)
        tail = lax.slice_in_dim(cells, cells.shape[dim] - width, cells.shape[dim], axis=dim)
        cells = jnp.concatenate(
            [
                lax.ppermute(tail, axis, [(i, (i + 1) % count) for i in range(ends)]),
                cells,
                lax.ppermute(head, axis, [((i + 1) % count, i) for i in range(ends)]),
            ],
            axis=dim,
        )
    return cells


AXES = ("gx", "gy", "gz")
HALO_Z = 8


def assemble_padded(padded):
    for direction_index in range(1, 4):
        padded = pair_pass(padded, direction_index)
    return padded[:, 1:-1, 1:-1, 1:-1]


def assemble_many(stack):
    return assemble_padded(extended(stack, (("gx", 1), ("gy", 2), ("gz", 3)), 1))


def ring_gather(block, axis, count, dim):
    assert count & (count - 1) == 0
    have = block
    step = 1
    while step < count:
        came = lax.ppermute(have, axis, [(i, (i + step) % count) for i in range(count)])
        have = jnp.concatenate([came, have], axis=dim)
        step *= 2
    width = block.shape[dim]
    shift = (lax.axis_index(axis) + 1) * width
    doubled = jnp.concatenate([have, have], axis=dim)
    start = [0] * have.ndim
    start[dim] = count * width - shift
    return lax.dynamic_slice(doubled, start, have.shape)


def gather_coarse(values, sizes):
    full = ring_gather(values, "gx", sizes[0], 0)
    full = ring_gather(full, "gy", sizes[1], 1)
    count = sizes[2]
    depth = full.shape[2]
    assert HALO_Z <= depth
    head = full[:, :, :HALO_Z]
    tail = full[:, :, depth - HALO_Z :]
    low = lax.ppermute(tail, "gz", [(i, i + 1) for i in range(count - 1)])
    high = lax.ppermute(head, "gz", [(i + 1, i) for i in range(count - 1)])
    return jnp.concatenate([low, full, high], axis=2)


def shards(sizes):
    def body(
        thermal_state_values,
        flow_speed_components,
        thermal_diffusivity_coefficient,
        specific_volume,
        lower_level_helmholtz_offset,
    ):
        derivs, weights = gll_tables()
        length_along_x, length_along_y, length_along_z = thermal_state_values.shape
        blocks_x, blocks_y, blocks_z = lower_level_helmholtz_offset.shape
        interpolation_apply = make_pair(derivs, length_along_z)
        adjoint_interpolation = make_pair(derivs.T, length_along_z)
        square_back = make_pair((derivs * derivs).T, length_along_z)
        cube_w = weight_cube(weights)
        quadrature_coefficient = jnp.tile(cube_w, (blocks_x, blocks_y, blocks_z))

        def assemble_one(values):
            return assemble_many(values[None])[0]

        helm_full = gather_coarse(lower_level_helmholtz_offset, sizes)
        ix = lax.axis_index("gx")
        iy = lax.axis_index("gy")
        iz = lax.axis_index("gz")
        cell_z = lax.broadcasted_iota(jnp.int32, helm_full.shape, 2) + (iz * blocks_z - HALO_Z)
        inside = ((cell_z >= 0) & (cell_z < sizes[2] * blocks_z)).astype(jnp.float32)

        def padded_weights(length):
            return weights[np.arange(7, 7 + length + 2) % 8]

        w_pad = (
            padded_weights(length_along_x)[:, None, None]
            * padded_weights(length_along_y)[None, :, None]
        ) * padded_weights(length_along_z)[None, None, :]

        def assemble_from_coarse(coarse_full):
            coarse_pad = jnp.pad(coarse_full, ((1, 1), (1, 1), (0, 0)))
            window = lax.dynamic_slice(
                coarse_pad,
                (ix * blocks_x, iy * blocks_y, HALO_Z - 1),
                (blocks_x + 2, blocks_y + 2, blocks_z + 2),
            )
            nodes = jnp.repeat(jnp.repeat(jnp.repeat(window, 8, 0), 8, 1), 8, 2)
            nodes = nodes[
                7 : 7 + length_along_x + 2, 7 : 7 + length_along_y + 2, 7 : 7 + length_along_z + 2
            ]
            return assemble_padded((w_pad * nodes)[None])[0]

        quadrature_lumped_matrix = assemble_from_coarse(inside)

        partial_derivative_stack = [
            apply_derivative_matrix(thermal_state_values, interpolation_apply, direction_index)
            for direction_index in range(3)
        ]
        advect = (
            flow_speed_components[0] * partial_derivative_stack[0]
            + flow_speed_components[1] * partial_derivative_stack[1]
            + flow_speed_components[2] * partial_derivative_stack[2]
        )
        diffuse = apply_derivative_matrix(
            quadrature_coefficient * thermal_diffusivity_coefficient * partial_derivative_stack[0],
            adjoint_interpolation,
            0,
        )
        diffuse = diffuse + apply_derivative_matrix(
            quadrature_coefficient * thermal_diffusivity_coefficient * partial_derivative_stack[1],
            adjoint_interpolation,
            1,
        )
        diffuse = diffuse + apply_derivative_matrix(
            quadrature_coefficient * thermal_diffusivity_coefficient * partial_derivative_stack[2],
            adjoint_interpolation,
            2,
        )
        heat_local = -(quadrature_coefficient * advect) - diffuse
        coef_w = quadrature_coefficient * specific_volume
        jacobi_local = (
            apply_derivative_matrix(coef_w, square_back, 0)
            + apply_derivative_matrix(coef_w, square_back, 1)
            + apply_derivative_matrix(coef_w, square_back, 2)
            + HELM_SHIFT * quadrature_coefficient
        )
        both = assemble_many(jnp.stack([heat_local, jacobi_local]))
        volumetric_source_strength = both[0]
        jacobi = both[1]
        updated_thermal_state = (
            thermal_state_values
            + CLOCK_STEP_SIZE * volumetric_source_strength / quadrature_lumped_matrix
        )
        boundary_heat_outflow = apply_derivative_matrix(
            quadrature_coefficient * flow_speed_components[0], adjoint_interpolation, 0
        ) + apply_derivative_matrix(
            quadrature_coefficient * flow_speed_components[1], adjoint_interpolation, 1
        )
        boundary_heat_outflow = boundary_heat_outflow + apply_derivative_matrix(
            quadrature_coefficient * (flow_speed_components[2] + updated_thermal_state),
            adjoint_interpolation,
            2,
        )
        right_side = assemble_one(boundary_heat_outflow)
        inv_jac = 1.0 / jacobi

        def apply_fine(values):
            local_k = apply_derivative_matrix(
                coef_w * apply_derivative_matrix(values, interpolation_apply, 0),
                adjoint_interpolation,
                0,
            )
            local_k = local_k + apply_derivative_matrix(
                coef_w * apply_derivative_matrix(values, interpolation_apply, 1),
                adjoint_interpolation,
                1,
            )
            local_k = local_k + apply_derivative_matrix(
                coef_w * apply_derivative_matrix(values, interpolation_apply, 2),
                adjoint_interpolation,
                2,
            )
            return assemble_one(local_k + HELM_SHIFT * quadrature_coefficient * values)

        def apply_coarse(values):
            return inside * stencil(jnp.pad(values, 1), helm_full)

        coarse_inv = 1.0 / (6.0 + helm_full)
        row_ids = lax.broadcasted_iota(jnp.int32, (length_along_z, blocks_z), 0) // 8
        col_ids = lax.broadcasted_iota(jnp.int32, (length_along_z, blocks_z), 1)
        summer = jnp.where(row_ids == col_ids, 1.0, 0.0).astype(jnp.float32)
        pressure_iterate_values = jnp.zeros_like(thermal_state_values)
        equation_misfit = right_side
        for iter_no in range(PITERS):
            smooth, resid_s = chebyshev(
                equation_misfit, apply_fine, inv_jac, FINE_LOW, FINE_HIGH, SMOOTH, True
            )
            along_z = jnp.dot(
                (quadrature_coefficient * resid_s).reshape(
                    length_along_x * length_along_y, length_along_z
                ),
                summer,
                precision=lax.Precision.HIGHEST,
            )
            coarse_r = along_z.reshape(blocks_x, 8, blocks_y, 8, blocks_z).sum(axis=(1, 3)) / 8.0
            coarse_full = gather_coarse(coarse_r, sizes)
            correct, unused = chebyshev(
                coarse_full, apply_coarse, coarse_inv, COARSE_LOW, COARSE_HIGH, CHEB_C, False
            )
            prolong = assemble_from_coarse(correct) / quadrature_lumped_matrix
            pressure_iterate_values = pressure_iterate_values + smooth + prolong
            equation_misfit = resid_s - apply_fine(prolong)
        return (updated_thermal_state, pressure_iterate_values, equation_misfit)

    return body


def solution(mesh):
    sizes = tuple(mesh.shape[name] for name in AXES)
    in_specs = (
        P("gx", "gy", "gz"),
        P(None, "gx", "gy", "gz"),
        P("gx", "gy", "gz"),
        P("gx", "gy", "gz"),
        P("gx", "gy", "gz"),
    )
    out_specs = (P("gx", "gy", "gz"), P("gx", "gy", "gz"), P("gx", "gy", "gz"))
    return jax.shard_map(
        shards(sizes), mesh=mesh, in_specs=in_specs, out_specs=out_specs, check_vma=False
    )
```

```python
import jax
import jax.numpy as jnp
from jax import lax
from jax.sharding import PartitionSpec as P
import numpy as np

PITERS = 2
SMOOTH = 3
CHEB_C = 8


CLOCK_STEP_SIZE = 0.0002
HELM_SHIFT = 1.0
FINE_LOW = 0.25
FINE_HIGH = 3.0
COARSE_LOW = 0.07
COARSE_HIGH = 2.0
GLL_POINTS = (
    -1.0,
    -0.8717401485096066,
    -0.5917001814331423,
    -0.2092992179024789,
    0.0,
    0.2092992179024789,
    0.5917001814331423,
    0.8717401485096066,
    1.0,
)


def legendre_seven(point):
    p_prev = 1.0
    p_cur = point
    for order_k in range(1, 7):
        p_next = ((2.0 * order_k + 1.0) * point * p_cur - order_k * p_prev) / (order_k + 1.0)
        p_prev = p_cur
        p_cur = p_next
    return p_cur


def gll_tables():
    degree_n = 7
    points = list(GLL_POINTS[:4] + GLL_POINTS[5:])
    legend = [legendre_seven(point) for point in points]
    weights = [2.0 / (degree_n * (degree_n + 1) * value * value) for value in legend]
    derivs = []
    for row_no in range(8):
        row_vals = []
        for col_no in range(8):
            if row_no != col_no:
                row_vals.append(
                    legend[row_no] / (legend[col_no] * (points[row_no] - points[col_no]))
                )
            else:
                row_vals.append(0.0)
        derivs.append(row_vals)
    derivs[0][0] = -degree_n * (degree_n + 1) / 4.0
    derivs[7][7] = degree_n * (degree_n + 1) / 4.0
    return (jnp.asarray(derivs, jnp.float32), jnp.asarray(weights, jnp.float32))


def weight_cube(weights):
    return weights[:, None, None] * weights[None, :, None] * weights[None, None, :]


def pair_pass(padded, direction_index):
    extent = padded.shape[direction_index]
    zero_rim = jnp.zeros_like(lax.slice_in_dim(padded, 0, 1, axis=direction_index))
    shifted_up = jnp.concatenate(
        [lax.slice_in_dim(padded, 1, extent, axis=direction_index), zero_rim], axis=direction_index
    )
    shifted_down = jnp.concatenate(
        [zero_rim, lax.slice_in_dim(padded, 0, extent - 1, axis=direction_index)],
        axis=direction_index,
    )
    position = lax.broadcasted_iota(jnp.int32, padded.shape, direction_index) % 8
    return (
        padded
        + jnp.where(position == 0, shifted_up, 0.0)
        + jnp.where(position == 1, shifted_down, 0.0)
    )


def make_pair(small_t, shape):
    length_along_x, length_along_y, length_along_z = shape

    def band(length):
        return jnp.kron(jnp.eye(length // 8, dtype=jnp.float32), small_t)

    return (band(length_along_x), band(length_along_y), band(length_along_z).T)


def apply_derivative_matrix(values, tables, direction_index):
    band_x, band_y, band_t = tables
    length_along_x, length_along_y, length_along_z = values.shape
    if direction_index == 0:
        result = jnp.dot(
            band_x,
            values.reshape(length_along_x, length_along_y * length_along_z),
            precision=lax.Precision.HIGHEST,
        )
        return result.reshape(values.shape)
    if direction_index == 1:
        return jnp.matmul(
            jnp.broadcast_to(band_y, (length_along_x, length_along_y, length_along_y)),
            values,
            precision=lax.Precision.HIGHEST,
        )
    result = jnp.dot(
        values.reshape(length_along_x * length_along_y, length_along_z),
        band_t,
        precision=lax.Precision.HIGHEST,
    )
    return result.reshape(values.shape)


def stencil(padded, shift_c):
    centre = padded[1:-1, 1:-1, 1:-1]
    beside_all = padded[2:, 1:-1, 1:-1] + padded[:-2, 1:-1, 1:-1]
    beside_all = beside_all + padded[1:-1, 2:, 1:-1] + padded[1:-1, :-2, 1:-1]
    beside_all = beside_all + padded[1:-1, 1:-1, 2:] + padded[1:-1, 1:-1, :-2]
    return (6.0 + shift_c) * centre - beside_all


def chebyshev(equation_misfit, apply_fn, inv_diag, low_end, high_end, sweeps, keep_resid):
    centre = 0.5 * (high_end + low_end)
    half_span = 0.5 * (high_end - low_end)
    span_ratio = centre / half_span
    rho_old = 1.0 / span_ratio
    direction = equation_misfit * inv_diag * (1.0 / centre)
    solution = direction
    for sweep_no in range(1, sweeps):
        equation_misfit = equation_misfit - apply_fn(direction)
        rho_new = 1.0 / (2.0 * span_ratio - rho_old)
        direction = rho_new * rho_old * direction + 2.0 * rho_new / half_span * (
            equation_misfit * inv_diag
        )
        solution = solution + direction
        rho_old = rho_new
    if keep_resid:
        equation_misfit = equation_misfit - apply_fn(direction)
    return (solution, equation_misfit)


def extended(cells, sides, width):
    for axis, dim in sides:
        count = lax.axis_size(axis)
        ends = count - 1
        head = lax.slice_in_dim(cells, 0, width, axis=dim)
        tail = lax.slice_in_dim(cells, cells.shape[dim] - width, cells.shape[dim], axis=dim)
        cells = jnp.concatenate(
            [
                lax.ppermute(tail, axis, [(i, (i + 1) % count) for i in range(ends)]),
                cells,
                lax.ppermute(head, axis, [((i + 1) % count, i) for i in range(ends)]),
            ],
            axis=dim,
        )
    return cells


AXES = ("gx", "gy", "gz")
HALO_Z = 8


def assemble_padded(padded):
    for direction_index in range(1, 4):
        padded = pair_pass(padded, direction_index)
    return padded[:, 1:-1, 1:-1, 1:-1]


def assemble_many(stack):
    return assemble_padded(extended(stack, (("gx", 1), ("gy", 2), ("gz", 3)), 1))


def ring_gather(block, axis, count, dim):
    assert count & (count - 1) == 0
    have = block
    step = 1
    while step < count:
        came = lax.ppermute(have, axis, [(i, (i + step) % count) for i in range(count)])
        have = jnp.concatenate([came, have], axis=dim)
        step *= 2
    width = block.shape[dim]
    shift = (lax.axis_index(axis) + 1) * width
    doubled = jnp.concatenate([have, have], axis=dim)
    start = [0] * have.ndim
    start[dim] = count * width - shift
    return lax.dynamic_slice(doubled, start, have.shape)


def gather_coarse(values, sizes):
    full = ring_gather(values, "gx", sizes[0], 0)
    full = ring_gather(full, "gy", sizes[1], 1)
    count = sizes[2]
    depth = full.shape[2]
    assert HALO_Z <= depth
    head = full[:, :, :HALO_Z]
    tail = full[:, :, depth - HALO_Z :]
    low = lax.ppermute(tail, "gz", [(i, i + 1) for i in range(count - 1)])
    high = lax.ppermute(head, "gz", [(i + 1, i) for i in range(count - 1)])
    return jnp.concatenate([low, full, high], axis=2)


def shards(sizes):
    def body(
        thermal_state_values,
        flow_speed_components,
        thermal_diffusivity_coefficient,
        specific_volume,
        lower_level_helmholtz_offset,
    ):
        derivs, weights = gll_tables()
        length_along_x, length_along_y, length_along_z = thermal_state_values.shape
        blocks_x, blocks_y, blocks_z = lower_level_helmholtz_offset.shape
        interpolation_apply = make_pair(derivs, thermal_state_values.shape)
        adjoint_interpolation = make_pair(derivs.T, thermal_state_values.shape)
        square_back = make_pair((derivs * derivs).T, thermal_state_values.shape)
        cube_w = weight_cube(weights)
        quadrature_coefficient = (
            jnp.tile(weights, blocks_x)[:, None, None] * jnp.tile(weights, blocks_y)[None, :, None]
        ) * jnp.tile(weights, blocks_z)[None, None, :]

        def assemble_one(values):
            return assemble_many(values[None])[0]

        helm_full = gather_coarse(lower_level_helmholtz_offset, sizes)
        ix = lax.axis_index("gx")
        iy = lax.axis_index("gy")
        iz = lax.axis_index("gz")
        cell_z = lax.broadcasted_iota(jnp.int32, helm_full.shape, 2) + (iz * blocks_z - HALO_Z)
        inside = ((cell_z >= 0) & (cell_z < sizes[2] * blocks_z)).astype(jnp.float32)

        def padded_weights(length):
            return weights[np.arange(7, 7 + length + 2) % 8]

        w_pad = (
            padded_weights(length_along_x)[:, None, None]
            * padded_weights(length_along_y)[None, :, None]
        ) * padded_weights(length_along_z)[None, None, :]

        def assemble_from_coarse(coarse_full):
            coarse_pad = jnp.pad(coarse_full, ((1, 1), (1, 1), (0, 0)))
            window = lax.dynamic_slice(
                coarse_pad,
                (ix * blocks_x, iy * blocks_y, HALO_Z - 1),
                (blocks_x + 2, blocks_y + 2, blocks_z + 2),
            )
            nodes = jnp.repeat(jnp.repeat(jnp.repeat(window, 8, 0), 8, 1), 8, 2)
            nodes = nodes[
                7 : 7 + length_along_x + 2, 7 : 7 + length_along_y + 2, 7 : 7 + length_along_z + 2
            ]
            return assemble_padded((w_pad * nodes)[None])[0]

        quadrature_lumped_matrix = assemble_from_coarse(inside)

        partial_derivative_stack = [
            apply_derivative_matrix(thermal_state_values, interpolation_apply, direction_index)
            for direction_index in range(3)
        ]
        advect = (
            flow_speed_components[0] * partial_derivative_stack[0]
            + flow_speed_components[1] * partial_derivative_stack[1]
            + flow_speed_components[2] * partial_derivative_stack[2]
        )
        diffuse = apply_derivative_matrix(
            quadrature_coefficient * thermal_diffusivity_coefficient * partial_derivative_stack[0],
            adjoint_interpolation,
            0,
        )
        diffuse = diffuse + apply_derivative_matrix(
            quadrature_coefficient * thermal_diffusivity_coefficient * partial_derivative_stack[1],
            adjoint_interpolation,
            1,
        )
        diffuse = diffuse + apply_derivative_matrix(
            quadrature_coefficient * thermal_diffusivity_coefficient * partial_derivative_stack[2],
            adjoint_interpolation,
            2,
        )
        heat_local = -(quadrature_coefficient * advect) - diffuse
        coef_w = quadrature_coefficient * specific_volume
        jacobi_local = (
            apply_derivative_matrix(coef_w, square_back, 0)
            + apply_derivative_matrix(coef_w, square_back, 1)
            + apply_derivative_matrix(coef_w, square_back, 2)
            + HELM_SHIFT * quadrature_coefficient
        )
        both = assemble_many(jnp.stack([heat_local, jacobi_local]))
        volumetric_source_strength = both[0]
        jacobi = both[1]
        updated_thermal_state = (
            thermal_state_values
            + CLOCK_STEP_SIZE * volumetric_source_strength / quadrature_lumped_matrix
        )
        boundary_heat_outflow = apply_derivative_matrix(
            quadrature_coefficient * flow_speed_components[0], adjoint_interpolation, 0
        ) + apply_derivative_matrix(
            quadrature_coefficient * flow_speed_components[1], adjoint_interpolation, 1
        )
        boundary_heat_outflow = boundary_heat_outflow + apply_derivative_matrix(
            quadrature_coefficient * (flow_speed_components[2] + updated_thermal_state),
            adjoint_interpolation,
            2,
        )
        right_side = assemble_one(boundary_heat_outflow)
        inv_jac = 1.0 / jacobi

        def apply_fine(values):
            local_k = apply_derivative_matrix(
                coef_w * apply_derivative_matrix(values, interpolation_apply, 0),
                adjoint_interpolation,
                0,
            )
            local_k = local_k + apply_derivative_matrix(
                coef_w * apply_derivative_matrix(values, interpolation_apply, 1),
                adjoint_interpolation,
                1,
            )
            local_k = local_k + apply_derivative_matrix(
                coef_w * apply_derivative_matrix(values, interpolation_apply, 2),
                adjoint_interpolation,
                2,
            )
            return assemble_one(local_k + HELM_SHIFT * quadrature_coefficient * values)

        def apply_coarse(values):
            return inside * stencil(jnp.pad(values, 1), helm_full)

        coarse_inv = 1.0 / (6.0 + helm_full)
        row_ids = lax.broadcasted_iota(jnp.int32, (length_along_z, blocks_z), 0) // 8
        col_ids = lax.broadcasted_iota(jnp.int32, (length_along_z, blocks_z), 1)
        summer = jnp.where(row_ids == col_ids, 1.0, 0.0).astype(jnp.float32)
        pressure_iterate_values = jnp.zeros_like(thermal_state_values)
        equation_misfit = right_side
        for iter_no in range(PITERS):
            smooth, resid_s = chebyshev(
                equation_misfit, apply_fine, inv_jac, FINE_LOW, FINE_HIGH, SMOOTH, True
            )
            along_z = jnp.dot(
                (quadrature_coefficient * resid_s).reshape(
                    length_along_x * length_along_y, length_along_z
                ),
                summer,
                precision=lax.Precision.HIGHEST,
            )
            coarse_r = along_z.reshape(blocks_x, 8, blocks_y, 8, blocks_z).sum(axis=(1, 3)) / 8.0
            coarse_full = gather_coarse(coarse_r, sizes)
            correct, unused = chebyshev(
                coarse_full, apply_coarse, coarse_inv, COARSE_LOW, COARSE_HIGH, CHEB_C, False
            )
            prolong = assemble_from_coarse(correct) / quadrature_lumped_matrix
            pressure_iterate_values = pressure_iterate_values + smooth + prolong
            equation_misfit = resid_s - apply_fine(prolong)
        return (updated_thermal_state, pressure_iterate_values, equation_misfit)

    return body


def solution(mesh):
    sizes = tuple(mesh.shape[name] for name in AXES)
    in_specs = (
        P("gx", "gy", "gz"),
        P(None, "gx", "gy", "gz"),
        P("gx", "gy", "gz"),
        P("gx", "gy", "gz"),
        P("gx", "gy", "gz"),
    )
    out_specs = (P("gx", "gy", "gz"), P("gx", "gy", "gz"), P("gx", "gy", "gz"))
    return jax.shard_map(
        shards(sizes), mesh=mesh, in_specs=in_specs, out_specs=out_specs, check_vma=False
    )
```

```python
import jax
import jax.numpy as jnp
from jax import lax
from jax.sharding import PartitionSpec as P
import numpy as np

PITERS = 2
SMOOTH = 3
CHEB_C = 8


CLOCK_STEP_SIZE = 0.0002
HELM_SHIFT = 1.0
FINE_LOW = 0.25
FINE_HIGH = 3.0
COARSE_LOW = 0.07
COARSE_HIGH = 2.0
GLL_POINTS = (
    -1.0,
    -0.8717401485096066,
    -0.5917001814331423,
    -0.2092992179024789,
    0.0,
    0.2092992179024789,
    0.5917001814331423,
    0.8717401485096066,
    1.0,
)


def legendre_seven(point):
    p_prev = 1.0
    p_cur = point
    for order_k in range(1, 7):
        p_next = ((2.0 * order_k + 1.0) * point * p_cur - order_k * p_prev) / (order_k + 1.0)
        p_prev = p_cur
        p_cur = p_next
    return p_cur


def gll_tables():
    degree_n = 7
    points = list(GLL_POINTS[:4] + GLL_POINTS[5:])
    legend = [legendre_seven(point) for point in points]
    weights = [2.0 / (degree_n * (degree_n + 1) * value * value) for value in legend]
    derivs = []
    for row_no in range(8):
        row_vals = []
        for col_no in range(8):
            if row_no != col_no:
                row_vals.append(
                    legend[row_no] / (legend[col_no] * (points[row_no] - points[col_no]))
                )
            else:
                row_vals.append(0.0)
        derivs.append(row_vals)
    derivs[0][0] = -degree_n * (degree_n + 1) / 4.0
    derivs[7][7] = degree_n * (degree_n + 1) / 4.0
    return (jnp.asarray(derivs, jnp.float32), jnp.asarray(weights, jnp.float32))


def weight_cube(weights):
    return weights[:, None, None] * weights[None, :, None] * weights[None, None, :]


def pair_pass(padded, direction_index):
    extent = padded.shape[direction_index]
    zero_rim = jnp.zeros_like(lax.slice_in_dim(padded, 0, 1, axis=direction_index))
    shifted_up = jnp.concatenate(
        [lax.slice_in_dim(padded, 1, extent, axis=direction_index), zero_rim], axis=direction_index
    )
    shifted_down = jnp.concatenate(
        [zero_rim, lax.slice_in_dim(padded, 0, extent - 1, axis=direction_index)],
        axis=direction_index,
    )
    position = lax.broadcasted_iota(jnp.int32, padded.shape, direction_index) % 8
    return (
        padded
        + jnp.where(position == 0, shifted_up, 0.0)
        + jnp.where(position == 1, shifted_down, 0.0)
    )


def make_pair(small_t, shape):
    length_along_x, length_along_y, length_along_z = shape

    def band(length):
        return jnp.kron(jnp.eye(length // 8, dtype=jnp.float32), small_t)

    return (band(length_along_x), band(length_along_y), band(length_along_z).T)


def apply_derivative_matrix(values, tables, direction_index):
    band_x, band_y, band_t = tables
    length_along_x, length_along_y, length_along_z = values.shape
    if direction_index == 0:
        result = jnp.dot(
            band_x,
            values.reshape(length_along_x, length_along_y * length_along_z),
            precision=lax.Precision.HIGHEST,
        )
        return result.reshape(values.shape)
    if direction_index == 1:
        return jnp.matmul(
            jnp.broadcast_to(band_y, (length_along_x, length_along_y, length_along_y)),
            values,
            precision=lax.Precision.HIGHEST,
        )
    result = jnp.dot(
        values.reshape(length_along_x * length_along_y, length_along_z),
        band_t,
        precision=lax.Precision.HIGHEST,
    )
    return result.reshape(values.shape)


def stencil(padded, shift_c):
    centre = padded[1:-1, 1:-1, 1:-1]
    beside_all = padded[2:, 1:-1, 1:-1] + padded[:-2, 1:-1, 1:-1]
    beside_all = beside_all + padded[1:-1, 2:, 1:-1] + padded[1:-1, :-2, 1:-1]
    beside_all = beside_all + padded[1:-1, 1:-1, 2:] + padded[1:-1, 1:-1, :-2]
    return (6.0 + shift_c) * centre - beside_all


def chebyshev(equation_misfit, apply_fn, inv_diag, low_end, high_end, sweeps, keep_resid):
    centre = 0.5 * (high_end + low_end)
    half_span = 0.5 * (high_end - low_end)
    span_ratio = centre / half_span
    rho_old = 1.0 / span_ratio
    direction = equation_misfit * inv_diag * (1.0 / centre)
    solution = direction
    for sweep_no in range(1, sweeps):
        equation_misfit = equation_misfit - apply_fn(direction)
        rho_new = 1.0 / (2.0 * span_ratio - rho_old)
        direction = rho_new * rho_old * direction + 2.0 * rho_new / half_span * (
            equation_misfit * inv_diag
        )
        solution = solution + direction
        rho_old = rho_new
    if keep_resid:
        equation_misfit = equation_misfit - apply_fn(direction)
    return (solution, equation_misfit)


def extended(cells, sides, width):
    for axis, dim in sides:
        count = lax.axis_size(axis)
        ends = count - 1
        head = lax.slice_in_dim(cells, 0, width, axis=dim)
        tail = lax.slice_in_dim(cells, cells.shape[dim] - width, cells.shape[dim], axis=dim)
        cells = jnp.concatenate(
            [
                lax.ppermute(tail, axis, [(i, (i + 1) % count) for i in range(ends)]),
                cells,
                lax.ppermute(head, axis, [((i + 1) % count, i) for i in range(ends)]),
            ],
            axis=dim,
        )
    return cells


AXES = ("gx", "gy", "gz")
HALO_Z = 8


def assemble_padded(padded):
    for direction_index in range(1, 4):
        padded = pair_pass(padded, direction_index)
    return padded[:, 1:-1, 1:-1, 1:-1]


def assemble_many(stack):
    return assemble_padded(extended(stack, (("gx", 1), ("gy", 2), ("gz", 3)), 1))


def ring_gather(block, axis, count, dim):
    assert count & (count - 1) == 0
    have = block
    step = 1
    while step < count:
        came = lax.ppermute(have, axis, [(i, (i + step) % count) for i in range(count)])
        have = jnp.concatenate([came, have], axis=dim)
        step *= 2
    width = block.shape[dim]
    shift = (lax.axis_index(axis) + 1) * width
    doubled = jnp.concatenate([have, have], axis=dim)
    start = [0] * have.ndim
    start[dim] = count * width - shift
    return lax.dynamic_slice(doubled, start, have.shape)


def gather_coarse(values, sizes):
    full = ring_gather(values, "gx", sizes[0], 1)
    full = ring_gather(full, "gy", sizes[1], 2)
    count = sizes[2]
    depth = full.shape[3]
    assert HALO_Z <= depth
    head = full[:, :, :, :HALO_Z]
    tail = full[:, :, :, depth - HALO_Z :]
    low = lax.ppermute(tail, "gz", [(i, i + 1) for i in range(count - 1)])
    high = lax.ppermute(head, "gz", [(i + 1, i) for i in range(count - 1)])
    return jnp.concatenate([low, full, high], axis=3)


def shards(sizes):
    def body(
        thermal_state_values,
        flow_speed_components,
        thermal_diffusivity_coefficient,
        specific_volume,
        lower_level_helmholtz_offset,
    ):
        derivs, weights = gll_tables()
        length_along_x, length_along_y, length_along_z = thermal_state_values.shape
        blocks_x, blocks_y, blocks_z = lower_level_helmholtz_offset.shape
        interpolation_apply = make_pair(derivs, thermal_state_values.shape)
        adjoint_interpolation = make_pair(derivs.T, thermal_state_values.shape)
        square_back = make_pair((derivs * derivs).T, thermal_state_values.shape)
        cube_w = weight_cube(weights)
        quadrature_coefficient = (
            jnp.tile(weights, blocks_x)[:, None, None] * jnp.tile(weights, blocks_y)[None, :, None]
        ) * jnp.tile(weights, blocks_z)[None, None, :]

        def assemble_one(values):
            return assemble_many(values[None])[0]

        coarse_shape = (
            sizes[0] * blocks_x,
            sizes[1] * blocks_y,
            blocks_z + 2 * HALO_Z,
        )
        ix = lax.axis_index("gx")
        iy = lax.axis_index("gy")
        iz = lax.axis_index("gz")
        cell_z = lax.broadcasted_iota(jnp.int32, coarse_shape, 2) + (iz * blocks_z - HALO_Z)
        inside = ((cell_z >= 0) & (cell_z < sizes[2] * blocks_z)).astype(jnp.float32)

        def padded_weights(length):
            return weights[np.arange(7, 7 + length + 2) % 8]

        w_pad = (
            padded_weights(length_along_x)[:, None, None]
            * padded_weights(length_along_y)[None, :, None]
        ) * padded_weights(length_along_z)[None, None, :]

        def assemble_from_coarse(coarse_full):
            coarse_pad = jnp.pad(coarse_full, ((1, 1), (1, 1), (0, 0)))
            window = lax.dynamic_slice(
                coarse_pad,
                (ix * blocks_x, iy * blocks_y, HALO_Z - 1),
                (blocks_x + 2, blocks_y + 2, blocks_z + 2),
            )
            nodes = jnp.repeat(jnp.repeat(jnp.repeat(window, 8, 0), 8, 1), 8, 2)
            nodes = nodes[
                7 : 7 + length_along_x + 2, 7 : 7 + length_along_y + 2, 7 : 7 + length_along_z + 2
            ]
            return assemble_padded((w_pad * nodes)[None])[0]

        quadrature_lumped_matrix = assemble_from_coarse(inside)

        partial_derivative_stack = [
            apply_derivative_matrix(thermal_state_values, interpolation_apply, direction_index)
            for direction_index in range(3)
        ]
        advect = (
            flow_speed_components[0] * partial_derivative_stack[0]
            + flow_speed_components[1] * partial_derivative_stack[1]
            + flow_speed_components[2] * partial_derivative_stack[2]
        )
        diffuse = apply_derivative_matrix(
            quadrature_coefficient * thermal_diffusivity_coefficient * partial_derivative_stack[0],
            adjoint_interpolation,
            0,
        )
        diffuse = diffuse + apply_derivative_matrix(
            quadrature_coefficient * thermal_diffusivity_coefficient * partial_derivative_stack[1],
            adjoint_interpolation,
            1,
        )
        diffuse = diffuse + apply_derivative_matrix(
            quadrature_coefficient * thermal_diffusivity_coefficient * partial_derivative_stack[2],
            adjoint_interpolation,
            2,
        )
        heat_local = -(quadrature_coefficient * advect) - diffuse
        coef_w = quadrature_coefficient * specific_volume
        jacobi_local = (
            apply_derivative_matrix(coef_w, square_back, 0)
            + apply_derivative_matrix(coef_w, square_back, 1)
            + apply_derivative_matrix(coef_w, square_back, 2)
            + HELM_SHIFT * quadrature_coefficient
        )
        both = assemble_many(jnp.stack([heat_local, jacobi_local]))
        volumetric_source_strength = both[0]
        jacobi = both[1]
        updated_thermal_state = (
            thermal_state_values
            + CLOCK_STEP_SIZE * volumetric_source_strength / quadrature_lumped_matrix
        )
        boundary_heat_outflow = apply_derivative_matrix(
            quadrature_coefficient * flow_speed_components[0], adjoint_interpolation, 0
        ) + apply_derivative_matrix(
            quadrature_coefficient * flow_speed_components[1], adjoint_interpolation, 1
        )
        boundary_heat_outflow = boundary_heat_outflow + apply_derivative_matrix(
            quadrature_coefficient * (flow_speed_components[2] + updated_thermal_state),
            adjoint_interpolation,
            2,
        )
        right_side = assemble_one(boundary_heat_outflow)
        inv_jac = 1.0 / jacobi

        def apply_fine(values):
            local_k = apply_derivative_matrix(
                coef_w * apply_derivative_matrix(values, interpolation_apply, 0),
                adjoint_interpolation,
                0,
            )
            local_k = local_k + apply_derivative_matrix(
                coef_w * apply_derivative_matrix(values, interpolation_apply, 1),
                adjoint_interpolation,
                1,
            )
            local_k = local_k + apply_derivative_matrix(
                coef_w * apply_derivative_matrix(values, interpolation_apply, 2),
                adjoint_interpolation,
                2,
            )
            return assemble_one(local_k + HELM_SHIFT * quadrature_coefficient * values)

        row_ids = lax.broadcasted_iota(jnp.int32, (length_along_z, blocks_z), 0) // 8
        col_ids = lax.broadcasted_iota(jnp.int32, (length_along_z, blocks_z), 1)
        summer = jnp.where(row_ids == col_ids, 1.0, 0.0).astype(jnp.float32)
        pressure_iterate_values = jnp.zeros_like(thermal_state_values)
        equation_misfit = right_side
        for iter_no in range(PITERS):
            smooth, resid_s = chebyshev(
                equation_misfit, apply_fine, inv_jac, FINE_LOW, FINE_HIGH, SMOOTH, True
            )
            along_z = jnp.dot(
                (quadrature_coefficient * resid_s).reshape(
                    length_along_x * length_along_y, length_along_z
                ),
                summer,
                precision=lax.Precision.HIGHEST,
            )
            coarse_r = along_z.reshape(blocks_x, 8, blocks_y, 8, blocks_z).sum(axis=(1, 3)) / 8.0
            if iter_no == 0:
                gathered = gather_coarse(jnp.stack([coarse_r, lower_level_helmholtz_offset]), sizes)
                coarse_full = gathered[0]
                helm_full = gathered[1]
                coarse_inv = 1.0 / (6.0 + helm_full)

                def apply_coarse(values):
                    return inside * stencil(jnp.pad(values, 1), helm_full)

            else:
                coarse_full = gather_coarse(coarse_r[None], sizes)[0]
            correct, unused = chebyshev(
                coarse_full, apply_coarse, coarse_inv, COARSE_LOW, COARSE_HIGH, CHEB_C, False
            )
            prolong = assemble_from_coarse(correct) / quadrature_lumped_matrix
            pressure_iterate_values = pressure_iterate_values + smooth + prolong
            equation_misfit = resid_s - apply_fine(prolong)
        return (updated_thermal_state, pressure_iterate_values, equation_misfit)

    return body


def solution(mesh):
    sizes = tuple(mesh.shape[name] for name in AXES)
    in_specs = (
        P("gx", "gy", "gz"),
        P(None, "gx", "gy", "gz"),
        P("gx", "gy", "gz"),
        P("gx", "gy", "gz"),
        P("gx", "gy", "gz"),
    )
    out_specs = (P("gx", "gy", "gz"), P("gx", "gy", "gz"), P("gx", "gy", "gz"))
    return jax.shard_map(
        shards(sizes), mesh=mesh, in_specs=in_specs, out_specs=out_specs, check_vma=False
    )
```

```python
import jax
import jax.numpy as jnp
from jax import lax
from jax.sharding import PartitionSpec as P
import numpy as np

PITERS = 2
SMOOTH = 3
CHEB_C = 8


CLOCK_STEP_SIZE = 0.0002
HELM_SHIFT = 1.0
FINE_LOW = 0.25
FINE_HIGH = 3.0
COARSE_LOW = 0.07
COARSE_HIGH = 2.0
GLL_POINTS = (
    -1.0,
    -0.8717401485096066,
    -0.5917001814331423,
    -0.2092992179024789,
    0.0,
    0.2092992179024789,
    0.5917001814331423,
    0.8717401485096066,
    1.0,
)


def legendre_seven(point):
    p_prev = 1.0
    p_cur = point
    for order_k in range(1, 7):
        p_next = ((2.0 * order_k + 1.0) * point * p_cur - order_k * p_prev) / (order_k + 1.0)
        p_prev = p_cur
        p_cur = p_next
    return p_cur


def gll_tables():
    degree_n = 7
    points = list(GLL_POINTS[:4] + GLL_POINTS[5:])
    legend = [legendre_seven(point) for point in points]
    weights = [2.0 / (degree_n * (degree_n + 1) * value * value) for value in legend]
    derivs = []
    for row_no in range(8):
        row_vals = []
        for col_no in range(8):
            if row_no != col_no:
                row_vals.append(
                    legend[row_no] / (legend[col_no] * (points[row_no] - points[col_no]))
                )
            else:
                row_vals.append(0.0)
        derivs.append(row_vals)
    derivs[0][0] = -degree_n * (degree_n + 1) / 4.0
    derivs[7][7] = degree_n * (degree_n + 1) / 4.0
    return (jnp.asarray(derivs, jnp.float32), jnp.asarray(weights, jnp.float32))


def weight_cube(weights):
    return weights[:, None, None] * weights[None, :, None] * weights[None, None, :]


def pair_pass(padded, direction_index):
    extent = padded.shape[direction_index]
    zero_rim = jnp.zeros_like(lax.slice_in_dim(padded, 0, 1, axis=direction_index))
    shifted_up = jnp.concatenate(
        [lax.slice_in_dim(padded, 1, extent, axis=direction_index), zero_rim], axis=direction_index
    )
    shifted_down = jnp.concatenate(
        [zero_rim, lax.slice_in_dim(padded, 0, extent - 1, axis=direction_index)],
        axis=direction_index,
    )
    position = lax.broadcasted_iota(jnp.int32, padded.shape, direction_index) % 8
    return (
        padded
        + jnp.where(position == 0, shifted_up, 0.0)
        + jnp.where(position == 1, shifted_down, 0.0)
    )


def make_pair(small_t, shape):
    length_along_x, length_along_y, length_along_z = shape

    def band(length):
        return jnp.kron(jnp.eye(length // 8, dtype=jnp.float32), small_t)

    return (band(length_along_x), band(length_along_y), band(length_along_z).T)


def apply_derivative_matrix(values, tables, direction_index):
    band_x, band_y, band_t = tables
    length_along_x, length_along_y, length_along_z = values.shape
    if direction_index == 0:
        result = jnp.dot(
            band_x,
            values.reshape(length_along_x, length_along_y * length_along_z),
            precision=lax.Precision.HIGHEST,
        )
        return result.reshape(values.shape)
    if direction_index == 1:
        return jnp.matmul(
            jnp.broadcast_to(band_y, (length_along_x, length_along_y, length_along_y)),
            values,
            precision=lax.Precision.HIGHEST,
        )
    result = jnp.dot(
        values.reshape(length_along_x * length_along_y, length_along_z),
        band_t,
        precision=lax.Precision.HIGHEST,
    )
    return result.reshape(values.shape)


def stencil(padded, shift_c):
    centre = padded[1:-1, 1:-1, 1:-1]
    beside_all = padded[2:, 1:-1, 1:-1] + padded[:-2, 1:-1, 1:-1]
    beside_all = beside_all + padded[1:-1, 2:, 1:-1] + padded[1:-1, :-2, 1:-1]
    beside_all = beside_all + padded[1:-1, 1:-1, 2:] + padded[1:-1, 1:-1, :-2]
    return (6.0 + shift_c) * centre - beside_all


def chebyshev(equation_misfit, apply_fn, inv_diag, low_end, high_end, sweeps, keep_resid):
    centre = 0.5 * (high_end + low_end)
    half_span = 0.5 * (high_end - low_end)
    span_ratio = centre / half_span
    rho_old = 1.0 / span_ratio
    direction = equation_misfit * inv_diag * (1.0 / centre)
    solution = direction
    for sweep_no in range(1, sweeps):
        equation_misfit = equation_misfit - apply_fn(direction)
        rho_new = 1.0 / (2.0 * span_ratio - rho_old)
        direction = rho_new * rho_old * direction + 2.0 * rho_new / half_span * (
            equation_misfit * inv_diag
        )
        solution = solution + direction
        rho_old = rho_new
    if keep_resid:
        equation_misfit = equation_misfit - apply_fn(direction)
    return (solution, equation_misfit)


def extended(cells, sides, width):
    for axis, dim in sides:
        count = lax.axis_size(axis)
        ends = count - 1
        head = lax.slice_in_dim(cells, 0, width, axis=dim)
        tail = lax.slice_in_dim(cells, cells.shape[dim] - width, cells.shape[dim], axis=dim)
        cells = jnp.concatenate(
            [
                lax.ppermute(tail, axis, [(i, (i + 1) % count) for i in range(ends)]),
                cells,
                lax.ppermute(head, axis, [((i + 1) % count, i) for i in range(ends)]),
            ],
            axis=dim,
        )
    return cells


AXES = ("gx", "gy", "gz")
HALO_Z = 8


def assemble_padded(padded):
    for direction_index in range(1, 4):
        padded = pair_pass(padded, direction_index)
    return padded[:, 1:-1, 1:-1, 1:-1]


def assemble_many(stack):
    return assemble_padded(extended(stack, (("gz", 3), ("gy", 2), ("gx", 1)), 1))


def ring_gather(block, axis, count, dim):
    assert count & (count - 1) == 0
    have = block
    step = 1
    while step < count:
        came = lax.ppermute(have, axis, [(i, (i + step) % count) for i in range(count)])
        have = jnp.concatenate([came, have], axis=dim)
        step *= 2
    width = block.shape[dim]
    shift = (lax.axis_index(axis) + 1) * width
    doubled = jnp.concatenate([have, have], axis=dim)
    start = [0] * have.ndim
    start[dim] = count * width - shift
    return lax.dynamic_slice(doubled, start, have.shape)


def gather_coarse(values, sizes):
    full = ring_gather(values, "gx", sizes[0], 0)
    full = ring_gather(full, "gy", sizes[1], 1)
    count = sizes[2]
    depth = full.shape[2]
    assert HALO_Z <= depth
    head = full[:, :, :HALO_Z]
    tail = full[:, :, depth - HALO_Z :]
    low = lax.ppermute(tail, "gz", [(i, i + 1) for i in range(count - 1)])
    high = lax.ppermute(head, "gz", [(i + 1, i) for i in range(count - 1)])
    return jnp.concatenate([low, full, high], axis=2)


def shards(sizes):
    def body(
        thermal_state_values,
        flow_speed_components,
        thermal_diffusivity_coefficient,
        specific_volume,
        lower_level_helmholtz_offset,
    ):
        derivs, weights = gll_tables()
        length_along_x, length_along_y, length_along_z = thermal_state_values.shape
        blocks_x, blocks_y, blocks_z = lower_level_helmholtz_offset.shape
        interpolation_apply = make_pair(derivs, thermal_state_values.shape)
        adjoint_interpolation = make_pair(derivs.T, thermal_state_values.shape)
        square_back = make_pair((derivs * derivs).T, thermal_state_values.shape)
        cube_w = weight_cube(weights)
        quadrature_coefficient = (
            jnp.tile(weights, blocks_x)[:, None, None] * jnp.tile(weights, blocks_y)[None, :, None]
        ) * jnp.tile(weights, blocks_z)[None, None, :]

        def assemble_one(values):
            return assemble_many(values[None])[0]

        helm_full = gather_coarse(lower_level_helmholtz_offset, sizes)
        ix = lax.axis_index("gx")
        iy = lax.axis_index("gy")
        iz = lax.axis_index("gz")
        cell_z = lax.broadcasted_iota(jnp.int32, helm_full.shape, 2) + (iz * blocks_z - HALO_Z)
        inside = ((cell_z >= 0) & (cell_z < sizes[2] * blocks_z)).astype(jnp.float32)

        def padded_weights(length):
            return weights[np.arange(7, 7 + length + 2) % 8]

        w_pad = (
            padded_weights(length_along_x)[:, None, None]
            * padded_weights(length_along_y)[None, :, None]
        ) * padded_weights(length_along_z)[None, None, :]

        def assemble_from_coarse(coarse_full):
            coarse_pad = jnp.pad(coarse_full, ((1, 1), (1, 1), (0, 0)))
            window = lax.dynamic_slice(
                coarse_pad,
                (ix * blocks_x, iy * blocks_y, HALO_Z - 1),
                (blocks_x + 2, blocks_y + 2, blocks_z + 2),
            )
            nodes = jnp.repeat(jnp.repeat(jnp.repeat(window, 8, 0), 8, 1), 8, 2)
            nodes = nodes[
                7 : 7 + length_along_x + 2, 7 : 7 + length_along_y + 2, 7 : 7 + length_along_z + 2
            ]
            return assemble_padded((w_pad * nodes)[None])[0]

        quadrature_lumped_matrix = assemble_from_coarse(inside)

        partial_derivative_stack = [
            apply_derivative_matrix(thermal_state_values, interpolation_apply, direction_index)
            for direction_index in range(3)
        ]
        advect = (
            flow_speed_components[0] * partial_derivative_stack[0]
            + flow_speed_components[1] * partial_derivative_stack[1]
            + flow_speed_components[2] * partial_derivative_stack[2]
        )
        diffuse = apply_derivative_matrix(
            quadrature_coefficient * thermal_diffusivity_coefficient * partial_derivative_stack[0],
            adjoint_interpolation,
            0,
        )
        diffuse = diffuse + apply_derivative_matrix(
            quadrature_coefficient * thermal_diffusivity_coefficient * partial_derivative_stack[1],
            adjoint_interpolation,
            1,
        )
        diffuse = diffuse + apply_derivative_matrix(
            quadrature_coefficient * thermal_diffusivity_coefficient * partial_derivative_stack[2],
            adjoint_interpolation,
            2,
        )
        heat_local = -(quadrature_coefficient * advect) - diffuse
        coef_w = quadrature_coefficient * specific_volume
        jacobi_local = (
            apply_derivative_matrix(coef_w, square_back, 0)
            + apply_derivative_matrix(coef_w, square_back, 1)
            + apply_derivative_matrix(coef_w, square_back, 2)
            + HELM_SHIFT * quadrature_coefficient
        )
        both = assemble_many(jnp.stack([heat_local, jacobi_local]))
        volumetric_source_strength = both[0]
        jacobi = both[1]
        updated_thermal_state = (
            thermal_state_values
            + CLOCK_STEP_SIZE * volumetric_source_strength / quadrature_lumped_matrix
        )
        boundary_heat_outflow = apply_derivative_matrix(
            quadrature_coefficient * flow_speed_components[0], adjoint_interpolation, 0
        ) + apply_derivative_matrix(
            quadrature_coefficient * flow_speed_components[1], adjoint_interpolation, 1
        )
        boundary_heat_outflow = boundary_heat_outflow + apply_derivative_matrix(
            quadrature_coefficient * (flow_speed_components[2] + updated_thermal_state),
            adjoint_interpolation,
            2,
        )
        right_side = assemble_one(boundary_heat_outflow)
        inv_jac = 1.0 / jacobi

        def apply_fine(values):
            local_k = apply_derivative_matrix(
                coef_w * apply_derivative_matrix(values, interpolation_apply, 0),
                adjoint_interpolation,
                0,
            )
            local_k = local_k + apply_derivative_matrix(
                coef_w * apply_derivative_matrix(values, interpolation_apply, 1),
                adjoint_interpolation,
                1,
            )
            local_k = local_k + apply_derivative_matrix(
                coef_w * apply_derivative_matrix(values, interpolation_apply, 2),
                adjoint_interpolation,
                2,
            )
            return assemble_one(local_k + HELM_SHIFT * quadrature_coefficient * values)

        def apply_coarse(values):
            return inside * stencil(jnp.pad(values, 1), helm_full)

        coarse_inv = 1.0 / (6.0 + helm_full)
        row_ids = lax.broadcasted_iota(jnp.int32, (length_along_z, blocks_z), 0) // 8
        col_ids = lax.broadcasted_iota(jnp.int32, (length_along_z, blocks_z), 1)
        summer = jnp.where(row_ids == col_ids, 1.0, 0.0).astype(jnp.float32)
        pressure_iterate_values = jnp.zeros_like(thermal_state_values)
        equation_misfit = right_side
        for iter_no in range(PITERS):
            smooth, resid_s = chebyshev(
                equation_misfit, apply_fine, inv_jac, FINE_LOW, FINE_HIGH, SMOOTH, True
            )
            along_z = jnp.dot(
                (quadrature_coefficient * resid_s).reshape(
                    length_along_x * length_along_y, length_along_z
                ),
                summer,
                precision=lax.Precision.HIGHEST,
            )
            coarse_r = along_z.reshape(blocks_x, 8, blocks_y, 8, blocks_z).sum(axis=(1, 3)) / 8.0
            coarse_full = gather_coarse(coarse_r, sizes)
            correct, unused = chebyshev(
                coarse_full, apply_coarse, coarse_inv, COARSE_LOW, COARSE_HIGH, CHEB_C, False
            )
            prolong = assemble_from_coarse(correct) / quadrature_lumped_matrix
            pressure_iterate_values = pressure_iterate_values + smooth + prolong
            equation_misfit = resid_s - apply_fine(prolong)
        return (updated_thermal_state, pressure_iterate_values, equation_misfit)

    return body


def solution(mesh):
    sizes = tuple(mesh.shape[name] for name in AXES)
    in_specs = (
        P("gx", "gy", "gz"),
        P(None, "gx", "gy", "gz"),
        P("gx", "gy", "gz"),
        P("gx", "gy", "gz"),
        P("gx", "gy", "gz"),
    )
    out_specs = (P("gx", "gy", "gz"), P("gx", "gy", "gz"), P("gx", "gy", "gz"))
    return jax.shard_map(
        shards(sizes), mesh=mesh, in_specs=in_specs, out_specs=out_specs, check_vma=False
    )
```
